256 devices in a mesh: users: 16 (over z, core), items: 16 (over y, x).
Axes of the slice: x: 4, y: 4, z: 8, core: 2. Of those that a mesh axis runs over, the one named last changes fastest.
Arguments:
- user_factors: float32 [16, 16, 512, 256], P('users', 'items'), may hold values from -0.5 to 0.5
- item_factor_blocks: float32 [16, 16, 256, 256], P('users', 'items'), may hold values from -0.5 to 0.5
- ratings: bfloat16 [16, 16, 8, 512, 256], P('users', 'items'), may hold values from -6 to 6
- rated_mask: int32 [16, 16, 8, 512, 256], P('users', 'items'), may hold values 0 or 1
- neighbor_offsets: int32 [16, 16, 4], P('users', 'items'), may hold values from -2 to 8, as said below
- neighbor_counts: int32 [16, 16], P('users', 'items'), may hold values from 1 to 4, as said below
- mix_tiles: float32 [16, 16, 4, 4, 128, 128], P('users', 'items'), may hold values from -0.5 to 0.5
- plan: int32 [8, 4], replicated, may hold values from 0 to 3, each once within a row
Outputs:
- users_out: float32 [16, 16, 512, 256], P('users', 'items')
- items_out: float32 [16, 16, 256, 256], P('users', 'items')
The draws below stay inside these ranges and needn't reach their ends.
Inputs may be any that keep to these rules, and one draw needn't show every extreme that they name: `neighbor_offsets`: each block's list holds the four distinct offsets -2, -1, 1 and 8 in some order; only the first neighbor_counts entries are used. `neighbor_counts`: some block uses all 4 entries.
All inputs are finite; a program needn't handle non-finite values. No bound on the sum of `rated_mask` on one device may be relied on, other than what follows from the above.
Results may differ from the reference program's by a relative error of at most 0.0003.
Values sent between devices are 32-bit elements; how exact they have to be, the bound alone decides.
No kernel may reach another device: no remote copies, remote signals or barrier semaphores. Data moves between devices by JAX's collectives and lax.ppermute only.
A program may use at most 128 MiB of HBM per device.

```python
import jax
import jax.numpy as jnp
from jax import lax

RANK = 256
USER_ROWS = 512
ITEM_ROWS = 256
TILE = 128
MAX_LINKS = 4
STOPS = 8
SUBS = 4
N_USERS = 16
N_ITEMS = 16


def factor_draw(key, shape):
    return jnp.clip(0.12 * jax.random.normal(key, shape, jnp.float32), -0.5, 0.5)


def draw_user_factors(key, part):
    return factor_draw(jax.random.fold_in(key, 11), (N_USERS, N_ITEMS, USER_ROWS, RANK))


def draw_item_factor_blocks(key, part):
    return factor_draw(jax.random.fold_in(key, 23), (N_USERS, N_ITEMS, ITEM_ROWS, RANK))


def neighbor_draw(key):
    base_key = jax.random.fold_in(key, 71)
    key_offsets, key_counts, key_full = jax.random.split(base_key, 3)
    scores = jax.random.randint(key_offsets, (N_USERS, N_ITEMS, MAX_LINKS), 0, 1000) * MAX_LINKS + jnp.arange(MAX_LINKS, dtype=jnp.int32)
    ordering = jnp.argsort(scores, axis=-1)
    value_lookup = jnp.array([-2, -1, 1, N_USERS // 2], dtype=jnp.int32)
    offsets = value_lookup[ordering]
    counts = jax.random.randint(key_counts, (N_USERS * N_ITEMS,), 1, MAX_LINKS + 1)
    full_block = jax.random.randint(key_full, (), 0, N_USERS * N_ITEMS)
    counts = jnp.where(jnp.arange(N_USERS * N_ITEMS) == full_block, MAX_LINKS, counts)
    return (offsets.astype(jnp.int32), counts.reshape(N_USERS, N_ITEMS).astype(jnp.int32))


def draw_neighbor_offsets(key, part):
    return neighbor_draw(key)[0]


def draw_neighbor_counts(key, part):
    return neighbor_draw(key)[1]


def set_ends(values, rng, low, top_value):
    longest = values.shape.index(max(values.shape))
    spots = []
    for shift in (0, 1):
        where = [jax.random.randint(jax.random.fold_in(rng, axis), (), 0, length) for axis, length in enumerate(values.shape)]
        where[longest] = (where[longest] + shift) % values.shape[longest]
        spots.append(tuple(where))
    return values.at[spots[0]].set(low).at[spots[1]].set(top_value)


def level_of(own_key, extent, cuts, smallest, top_value):
    loudness = 1.0
    for position, blocks in cuts:
        draws = jax.random.uniform(jax.random.fold_in(jax.random.fold_in(own_key, 6), position), (blocks,), jnp.float32, smallest / len(cuts), top_value / len(cuts))
        loudness = loudness * jnp.repeat(jnp.exp(draws), extent[position] // blocks).reshape((-1,) + (1,) * (len(extent) - 1 - position))
    return loudness


def scatter_about(stream_key, shape, scale, limit, shards=(), kind=jnp.bfloat16):
    gain = level_of(stream_key, shape, shards, -0.22, 0.18) if shards else 1.0
    result = jax.random.normal(stream_key, shape, jnp.float32) * scale * gain
    return jnp.minimum(jnp.maximum(result, -limit), limit).astype(kind)


def setup_inputs(seed: int = 0) -> dict:
    seeds = jax.random.split(jax.random.key(seed), 9)
    return {
        "user_factors": draw_user_factors(jax.random.fold_in(seeds[8], 71), 0),
        "item_factor_blocks": draw_item_factor_blocks(jax.random.fold_in(seeds[8], 71), 0),
        "ratings": scatter_about(seeds[2], (N_USERS, N_ITEMS, STOPS, USER_ROWS, ITEM_ROWS), 1.0, 6.0, ((0, 16), (1, 16))),
        "rated_mask": set_ends((jax.random.randint(seeds[3], (N_USERS, N_ITEMS, STOPS, USER_ROWS, ITEM_ROWS), 0, 2) < 1).astype(jnp.int32), jax.random.fold_in(seeds[3], 1), 0, 1),
        "neighbor_offsets": draw_neighbor_offsets(jax.random.fold_in(seeds[8], 71), 0),
        "neighbor_counts": draw_neighbor_counts(jax.random.fold_in(seeds[8], 71), 0),
        "mix_tiles": scatter_about(seeds[6], (N_USERS, N_ITEMS, MAX_LINKS, SUBS, TILE, TILE), TILE ** -0.5, 0.5, ((0, 16), (1, 16)), jnp.float32),
        "plan": jax.vmap(lambda own: jax.random.permutation(own, SUBS))(jax.random.split(seeds[7], STOPS)).reshape((STOPS, SUBS)).astype(jnp.int32),
    }


learning_rate = 0.025
graph_weight = 2.0


def graph_target(user_factors, neighbor_offsets, neighbor_counts, mix_tiles):
    sub_count = USER_ROWS // TILE
    group_index = jnp.arange(N_USERS, dtype=jnp.int32)[:, None]
    item_index = jnp.arange(N_ITEMS, dtype=jnp.int32)[None, :]
    total_sum = jnp.zeros((N_USERS, N_ITEMS, sub_count, TILE, RANK), jnp.float32)
    for slot_position in range(MAX_LINKS):
        source_group = (group_index + neighbor_offsets[:, :, slot_position]) % N_USERS
        blocks = user_factors[source_group, item_index].reshape(N_USERS, N_ITEMS, sub_count, TILE, RANK)
        mixed_rows = jnp.einsum("gisab,gisbr->gisar", mix_tiles[:, :, slot_position], blocks, precision=lax.Precision.HIGHEST)
        active_flag = (slot_position < neighbor_counts).astype(jnp.float32)[:, :, None, None, None]
        total_sum = total_sum + active_flag * mixed_rows
    total_sum = total_sum.reshape(N_USERS, N_ITEMS, USER_ROWS, RANK)
    return total_sum / neighbor_counts.astype(jnp.float32)[:, :, None, None]


def reference(user_factors, item_factor_blocks, ratings, rated_mask, neighbor_offsets, neighbor_counts, mix_tiles, plan):
    target = graph_target(user_factors, neighbor_offsets, neighbor_counts, mix_tiles)
    user_now = user_factors
    item_now = item_factor_blocks
    for stop_num in range(STOPS):
        if stop_num > 0:
            item_now = jnp.roll(item_now, 1, axis=1)
        for turn_num in range(USER_ROWS // TILE):
            row_start = (plan[stop_num, turn_num] * TILE).astype(jnp.int32)
            block_rows = lax.dynamic_slice_in_dim(user_now, row_start, TILE, 2)
            goal_rows = lax.dynamic_slice_in_dim(target, row_start, TILE, 2)
            rating_rows = lax.dynamic_slice_in_dim(ratings[:, :, stop_num], row_start, TILE, 2).astype(jnp.float32)
            observed = lax.dynamic_slice_in_dim(rated_mask[:, :, stop_num], row_start, TILE, 2).astype(jnp.float32)
            predicted = jnp.einsum("giar,gibr->giab", block_rows, item_now, precision=lax.Precision.HIGHEST)
            residual_err = observed * (predicted - rating_rows)
            grad_users = jnp.einsum("giab,gibr->giar", residual_err, item_now, precision=lax.Precision.HIGHEST) + graph_weight * (block_rows - goal_rows)
            grad_items = jnp.einsum("giab,giar->gibr", residual_err, block_rows, precision=lax.Precision.HIGHEST)
            user_now = lax.dynamic_update_slice_in_dim(user_now, block_rows - learning_rate * grad_users, row_start, 2)
            item_now = item_now - learning_rate * grad_items
    return user_now, item_now
```

```python
import functools

import jax
import jax.numpy as jnp
from jax import lax
from jax.experimental import pallas as pl
from jax.experimental.pallas import tpu as pltpu
from jax.sharding import PartitionSpec as P

TILE = 128
MAX_LINKS = 4
STOPS = 8


learning_rate = 0.025
graph_weight = 2.0
HI = lax.Precision.HIGHEST


def passed_along(value, axis, steps):
    count = lax.axis_size(axis)
    pairs = [(source, (source + steps) % count) for source in range(count)]
    return lax.ppermute(value, axis, pairs)


def stop_kernel(with_goal, plan_ref, u_ref, v_ref, q_ref, m_ref, *rest):
    if with_goal:
        g_ref, uo_ref, vo_ref = rest
    else:
        uo_ref, vo_ref = rest
    v = v_ref[...]
    for k in range(u_ref.shape[0] // TILE):
        s = pl.multiple_of(plan_ref[k] * TILE, TILE)
        b = u_ref[pl.ds(s, TILE), :]
        q = q_ref[pl.ds(s, TILE), :].astype(jnp.float32)
        m = m_ref[pl.ds(s, TILE), :].astype(jnp.float32)
        pred = lax.dot_general(
            b, v, (((1,), (1,)), ((), ())), precision=HI, preferred_element_type=jnp.float32
        )
        e = m * (pred - q)
        ev = jnp.dot(e, v, precision=HI, preferred_element_type=jnp.float32)
        gi = lax.dot_general(
            e, b, (((0,), (0,)), ((), ())), precision=HI, preferred_element_type=jnp.float32
        )
        if with_goal:
            g = g_ref[pl.ds(s, TILE), :]
            uo_ref[pl.ds(s, TILE), :] = b - learning_rate * (ev + graph_weight * (b - g))
        else:
            uo_ref[pl.ds(s, TILE), :] = b - learning_rate * (ev + graph_weight * b)
        v = v - learning_rate * gi
    vo_ref[...] = v


def run_stop(plan_row, user_now, item_now, stop_ratings, stop_mask, goal):
    with_goal = goal is not None
    rows, width = user_now.shape
    items = item_now.shape[0]
    operands = [plan_row, user_now, item_now, stop_ratings, stop_mask]
    if with_goal:
        operands.append(goal)
    vmem = pl.BlockSpec(memory_space=pltpu.VMEM)
    flops = 3 * 2 * rows * items * width
    return pl.pallas_call(
        functools.partial(stop_kernel, with_goal),
        out_shape=(
            jax.ShapeDtypeStruct((rows, width), jnp.float32),
            jax.ShapeDtypeStruct((items, width), jnp.float32),
        ),
        in_specs=[pl.BlockSpec(memory_space=pltpu.SMEM)] + [vmem] * (len(operands) - 1),
        out_specs=(vmem, vmem),
        cost_estimate=pl.CostEstimate(
            flops=6 * flops, transcendentals=0, bytes_accessed=4 * 4 * rows * width
        ),
    )(*operands)


def shards(
    user_factors,
    item_factor_blocks,
    ratings,
    rated_mask,
    neighbor_offsets,
    neighbor_counts,
    mix_tiles,
    plan,
):
    own_block = user_factors[0, 0]
    user_rows = own_block.shape[0]
    rank_width = own_block.shape[1]
    sub_count = user_rows // TILE
    offsets = neighbor_offsets[0, 0]
    count_used = neighbor_counts[0, 0]
    half_span = lax.axis_size("users") // 2
    far_block = passed_along(own_block, "users", -half_span)
    minus_two = passed_along(own_block, "users", 2)
    minus_one = passed_along(own_block, "users", 1)
    plus_one = passed_along(own_block, "users", -1)

    user_now, item_now = run_stop(
        plan[0], own_block, item_factor_blocks[0, 0], ratings[0, 0, 0], rated_mask[0, 0, 0], None
    )
    item_now = passed_along(item_now, "items", 1)

    stacked = jnp.stack([minus_two, minus_one, plus_one, far_block])
    position = jnp.where(offsets == half_span, 3, offsets + 2 - (offsets > 0).astype(jnp.int32))
    blocks = stacked[position]
    tile_collection = mix_tiles[0, 0]
    total_sum = jnp.zeros((sub_count, TILE, rank_width), jnp.float32)
    for slot_position in range(MAX_LINKS):
        adjacent_tile_rows = blocks[slot_position].reshape(sub_count, TILE, rank_width)
        mixed_rows = jnp.einsum(
            "gcj,gjz->gcz",
            tile_collection[slot_position],
            adjacent_tile_rows,
            precision=HI,
        )
        total_sum = total_sum + (slot_position < count_used).astype(jnp.float32) * mixed_rows
    target = total_sum.reshape(user_rows, rank_width) / count_used.astype(jnp.float32)
    user_now = user_now + (learning_rate * graph_weight) * target

    for stop_num in range(1, STOPS):
        user_now, item_now = run_stop(
            plan[stop_num],
            user_now,
            item_now,
            ratings[0, 0, stop_num],
            rated_mask[0, 0, stop_num],
            target,
        )
        if stop_num < STOPS - 1:
            item_now = passed_along(item_now, "items", 1)
    return (user_now[None, None], item_now[None, None])


def solution(mesh):
    return jax.shard_map(
        shards,
        mesh=mesh,
        in_specs=(
            P("users", "items", None, None),
            P("users", "items", None, None),
            P("users", "items", None, None, None),
            P("users", "items", None, None, None),
            P("users", "items", None),
            P("users", "items"),
            P("users", "items", None, None, None, None),
            P(),
        ),
        out_specs=(P("users", "items", None, None), P("users", "items", None, None)),
        check_vma=False,
    )
```

```python
import jax
import jax.numpy as jnp
from jax import lax
from jax.sharding import PartitionSpec as P

TILE = 128
MAX_LINKS = 4
STOPS = 8


learning_rate = 0.025
graph_weight = 2.0
HI = lax.Precision.HIGHEST


def passed_along(value, axis, steps):
    count = lax.axis_size(axis)
    pairs = [(source, (source + steps) % count) for source in range(count)]
    return lax.ppermute(value, axis, pairs)


def graph_target(own_block, offsets, count_used, tile_collection):
    user_rows, rank_width = own_block.shape
    sub_count = user_rows // TILE
    half_span = lax.axis_size("users") // 2
    far_block = passed_along(own_block, "users", -half_span)
    minus_two = passed_along(own_block, "users", 2)
    minus_one = passed_along(own_block, "users", 1)
    plus_one = passed_along(own_block, "users", -1)
    stacked = jnp.stack([minus_two, minus_one, plus_one, far_block])
    position = jnp.where(offsets == half_span, 3, offsets + 2 - (offsets > 0).astype(jnp.int32))
    blocks = stacked[position]
    total_sum = jnp.zeros((sub_count, TILE, rank_width), jnp.float32)
    for slot_position in range(MAX_LINKS):
        adjacent_tile_rows = blocks[slot_position].reshape(sub_count, TILE, rank_width)
        mixed_rows = jnp.einsum(
            "gcj,gjz->gcz",
            tile_collection[slot_position],
            adjacent_tile_rows,
            precision=HI,
        )
        total_sum = total_sum + (slot_position < count_used).astype(jnp.float32) * mixed_rows
    return total_sum / count_used.astype(jnp.float32)


def shards(
    user_factors,
    item_factor_blocks,
    ratings,
    rated_mask,
    neighbor_offsets,
    neighbor_counts,
    mix_tiles,
    plan,
):
    own_block = user_factors[0, 0]
    user_rows, rank_width = own_block.shape
    sub_count = user_rows // TILE
    target = graph_target(own_block, neighbor_offsets[0, 0], neighbor_counts[0, 0], mix_tiles[0, 0])
    tile_ids = jnp.arange(sub_count, dtype=jnp.int32)

    item_now = item_factor_blocks[0, 0]
    user_tiles = own_block.reshape(sub_count, TILE, rank_width)
    for stop_num in range(STOPS):
        order = plan[stop_num]
        slot_of = jnp.sum(
            jnp.where(order[None, :] == tile_ids[:, None], tile_ids[None, :], 0), axis=1
        )
        stop_ratings = ratings[0, 0, stop_num].reshape(sub_count, TILE, -1)
        stop_mask = rated_mask[0, 0, stop_num].reshape(sub_count, TILE, -1)
        rows = user_tiles[order]
        rating_rows = stop_ratings[order].astype(jnp.float32)
        observed = stop_mask[order].astype(jnp.float32)
        errors = []
        held = []
        for k in range(sub_count):
            block_rows = rows[k]
            predicted = lax.dot_general(
                block_rows, item_now, (((1,), (1,)), ((), ())), precision=HI
            )
            residual_err = observed[k] * (predicted - rating_rows[k])
            errors.append(residual_err)
            held.append(item_now)
            grad_items = lax.dot_general(
                residual_err, block_rows, (((0,), (0,)), ((), ())), precision=HI
            )
            item_now = item_now - learning_rate * grad_items
        if stop_num < STOPS - 1:
            item_now = passed_along(item_now, "items", 1)
        pulled = jnp.einsum(
            "kab,kbr->kar", jnp.stack(errors), jnp.stack(held), precision=HI
        )
        if stop_num == 0:
            updated = rows - learning_rate * (pulled + graph_weight * rows)
            user_tiles = updated[slot_of] + (learning_rate * graph_weight) * target
        else:
            updated = rows - learning_rate * (pulled + graph_weight * (rows - target[order]))
            user_tiles = updated[slot_of]
    user_now = user_tiles.reshape(user_rows, rank_width)
    return (user_now[None, None], item_now[None, None])


def solution(mesh):
    return jax.shard_map(
        shards,
        mesh=mesh,
        in_specs=(
            P("users", "items", None, None),
            P("users", "items", None, None),
            P("users", "items", None, None, None),
            P("users", "items", None, None, None),
            P("users", "items", None),
            P("users", "items"),
            P("users", "items", None, None, None, None),
            P(),
        ),
        out_specs=(P("users", "items", None, None), P("users", "items", None, None)),
        check_vma=False,
    )
```

```python
import jax
import jax.numpy as jnp
from jax import lax
from jax.sharding import PartitionSpec as P

TILE = 128
MAX_LINKS = 4
STOPS = 8
CHUNKS = 2


learning_rate = 0.025
graph_weight = 2.0
HI = lax.Precision.HIGHEST


def passed_along(value, axis, steps):
    count = lax.axis_size(axis)
    pairs = [(source, (source + steps) % count) for source in range(count)]
    return lax.ppermute(value, axis, pairs)


def chain_part(part, rows, ratings_cols, mask_cols, starts):
    errors = []
    held = []
    for k in range(len(rows)):
        block_rows = rows[k]
        rating_rows = lax.dynamic_slice_in_dim(ratings_cols, starts[k], TILE, 0).astype(jnp.float32)
        observed = lax.dynamic_slice_in_dim(mask_cols, starts[k], TILE, 0).astype(jnp.float32)
        predicted = lax.dot_general(block_rows, part, (((1,), (1,)), ((), ())), precision=HI)
        residual_err = observed * (predicted - rating_rows)
        errors.append(residual_err)
        held.append(part)
        grad_items = lax.dot_general(
            residual_err, block_rows, (((0,), (0,)), ((), ())), precision=HI
        )
        part = part - learning_rate * grad_items
    return part, errors, held


def graph_target(own_block, offsets, count_used, tile_collection):
    user_rows, rank_width = own_block.shape
    sub_count = user_rows // TILE
    half_span = lax.axis_size("users") // 2
    far_block = passed_along(own_block, "users", -half_span)
    minus_two = passed_along(own_block, "users", 2)
    minus_one = passed_along(own_block, "users", 1)
    plus_one = passed_along(own_block, "users", -1)
    stacked = jnp.stack([minus_two, minus_one, plus_one, far_block])
    position = jnp.where(offsets == half_span, 3, offsets + 2 - (offsets > 0).astype(jnp.int32))
    blocks = stacked[position]
    total_sum = jnp.zeros((sub_count, TILE, rank_width), jnp.float32)
    for slot_position in range(MAX_LINKS):
        adjacent_tile_rows = blocks[slot_position].reshape(sub_count, TILE, rank_width)
        mixed_rows = jnp.einsum(
            "gcj,gjz->gcz",
            tile_collection[slot_position],
            adjacent_tile_rows,
            precision=HI,
        )
        total_sum = total_sum + (slot_position < count_used).astype(jnp.float32) * mixed_rows
    return total_sum.reshape(user_rows, rank_width) / count_used.astype(jnp.float32)


def shards(
    user_factors,
    item_factor_blocks,
    ratings,
    rated_mask,
    neighbor_offsets,
    neighbor_counts,
    mix_tiles,
    plan,
):
    own_block = user_factors[0, 0]
    user_rows = own_block.shape[0]
    sub_count = user_rows // TILE
    target = graph_target(own_block, neighbor_offsets[0, 0], neighbor_counts[0, 0], mix_tiles[0, 0])

    item_block = item_factor_blocks[0, 0]
    width = item_block.shape[0] // CHUNKS
    user_now = own_block
    parts = [item_block[c * width:(c + 1) * width] for c in range(CHUNKS)]
    for stop_num in range(STOPS):
        stop_ratings = ratings[0, 0, stop_num]
        halting_mask = rated_mask[0, 0, stop_num]
        starts = [plan[stop_num, k] * TILE for k in range(sub_count)]
        rows = [lax.dynamic_slice_in_dim(user_now, s, TILE, 0) for s in starts]
        last = stop_num == STOPS - 1
        errors = []
        held = []
        for c in range(CHUNKS):
            cols = slice(c * width, (c + 1) * width)
            part, errs, hs = chain_part(
                parts[c], rows, stop_ratings[:, cols], halting_mask[:, cols], starts
            )
            errors.append(errs)
            held.append(hs)
            parts[c] = part if last else passed_along(part, "items", 1)
        for k in range(sub_count):
            block_rows = rows[k]
            grad_users = graph_weight * block_rows
            if stop_num > 0:
                grad_users = grad_users - graph_weight * lax.dynamic_slice_in_dim(
                    target, starts[k], TILE, 0
                )
            for c in range(CHUNKS):
                grad_users = grad_users + jnp.dot(errors[c][k], held[c][k], precision=HI)
            user_now = lax.dynamic_update_slice_in_dim(
                user_now, block_rows - learning_rate * grad_users, starts[k], 0
            )
        if stop_num == 0:
            user_now = user_now + (learning_rate * graph_weight) * target
    item_now = jnp.concatenate(parts, axis=0)
    return (user_now[None, None], item_now[None, None])


def solution(mesh):
    return jax.shard_map(
        shards,
        mesh=mesh,
        in_specs=(
            P("users", "items", None, None),
            P("users", "items", None, None),
            P("users", "items", None, None, None),
            P("users", "items", None, None, None),
            P("users", "items", None),
            P("users", "items"),
            P("users", "items", None, None, None, None),
            P(),
        ),
        out_specs=(P("users", "items", None, None), P("users", "items", None, None)),
        check_vma=False,
    )
```

```python
import jax
import jax.numpy as jnp
from jax import lax
from jax.sharding import PartitionSpec as P

TILE = 128
MAX_LINKS = 4
STOPS = 8
CHUNKS = 1


learning_rate = 0.025
graph_weight = 2.0
HI = lax.Precision.HIGHEST


def passed_along(value, axis, steps):
    count = lax.axis_size(axis)
    pairs = [(source, (source + steps) % count) for source in range(count)]
    return lax.ppermute(value, axis, pairs)


def chain_part(part, rows, ratings_cols, mask_cols, starts):
    errors = []
    held = []
    for k in range(len(rows)):
        block_rows = rows[k]
        rating_rows = lax.dynamic_slice_in_dim(ratings_cols, starts[k], TILE, 0).astype(jnp.float32)
        observed = lax.dynamic_slice_in_dim(mask_cols, starts[k], TILE, 0).astype(jnp.float32)
        predicted = lax.dot_general(block_rows, part, (((1,), (1,)), ((), ())), precision=HI)
        residual_err = observed * (predicted - rating_rows)
        errors.append(residual_err)
        held.append(part)
        grad_items = lax.dot_general(
            residual_err, block_rows, (((0,), (0,)), ((), ())), precision=HI
        )
        part = part - learning_rate * grad_items
    return part, errors, held


def graph_target(own_block, offsets, count_used, tile_collection):
    user_rows, rank_width = own_block.shape
    sub_count = user_rows // TILE
    half_span = lax.axis_size("users") // 2
    far_block = passed_along(own_block, "users", -half_span)
    minus_two = passed_along(own_block, "users", 2)
    minus_one = passed_along(own_block, "users", 1)
    plus_one = passed_along(own_block, "users", -1)
    stacked = jnp.stack([minus_two, minus_one, plus_one, far_block])
    position = jnp.where(offsets == half_span, 3, offsets + 2 - (offsets > 0).astype(jnp.int32))
    blocks = stacked[position]
    total_sum = jnp.zeros((sub_count, TILE, rank_width), jnp.float32)
    for slot_position in range(MAX_LINKS):
        adjacent_tile_rows = blocks[slot_position].reshape(sub_count, TILE, rank_width)
        mixed_rows = jnp.einsum(
            "gcj,gjz->gcz",
            tile_collection[slot_position],
            adjacent_tile_rows,
            precision=HI,
        )
        total_sum = total_sum + (slot_position < count_used).astype(jnp.float32) * mixed_rows
    return total_sum.reshape(user_rows, rank_width) / count_used.astype(jnp.float32)


def shards(
    user_factors,
    item_factor_blocks,
    ratings,
    rated_mask,
    neighbor_offsets,
    neighbor_counts,
    mix_tiles,
    plan,
):
    own_block = user_factors[0, 0]
    user_rows = own_block.shape[0]
    sub_count = user_rows // TILE
    target = graph_target(own_block, neighbor_offsets[0, 0], neighbor_counts[0, 0], mix_tiles[0, 0])

    item_block = item_factor_blocks[0, 0]
    width = item_block.shape[0] // CHUNKS
    user_now = own_block
    parts = [item_block[c * width:(c + 1) * width] for c in range(CHUNKS)]
    for stop_num in range(STOPS):
        stop_ratings = ratings[0, 0, stop_num]
        halting_mask = rated_mask[0, 0, stop_num]
        starts = [plan[stop_num, k] * TILE for k in range(sub_count)]
        rows = [lax.dynamic_slice_in_dim(user_now, s, TILE, 0) for s in starts]
        last = stop_num == STOPS - 1
        errors = []
        held = []
        for c in range(CHUNKS):
            cols = slice(c * width, (c + 1) * width)
            part, errs, hs = chain_part(
                parts[c], rows, stop_ratings[:, cols], halting_mask[:, cols], starts
            )
            errors.append(errs)
            held.append(hs)
            parts[c] = part if last else passed_along(part, "items", 1)
        for k in range(sub_count):
            block_rows = rows[k]
            grad_users = graph_weight * block_rows
            if stop_num > 0:
                grad_users = grad_users - graph_weight * lax.dynamic_slice_in_dim(
                    target, starts[k], TILE, 0
                )
            for c in range(CHUNKS):
                grad_users = grad_users + jnp.dot(errors[c][k], held[c][k], precision=HI)
            user_now = lax.dynamic_update_slice_in_dim(
                user_now, block_rows - learning_rate * grad_users, starts[k], 0
            )
        if stop_num == 0:
            user_now = user_now + (learning_rate * graph_weight) * target
    item_now = jnp.concatenate(parts, axis=0)
    return (user_now[None, None], item_now[None, None])


def solution(mesh):
    return jax.shard_map(
        shards,
        mesh=mesh,
        in_specs=(
            P("users", "items", None, None),
            P("users", "items", None, None),
            P("users", "items", None, None, None),
            P("users", "items", None, None, None),
            P("users", "items", None),
            P("users", "items"),
            P("users", "items", None, None, None, None),
            P(),
        ),
        out_specs=(P("users", "items", None, None), P("users", "items", None, None)),
        check_vma=False,
    )
```

```python
import jax
import jax.numpy as jnp
from jax import lax
from jax.sharding import PartitionSpec as P

TILE = 128
MAX_LINKS = 4
STOPS = 8
CHUNKS = 1


learning_rate = 0.025
graph_weight = 2.0
HI = lax.Precision.HIGHEST


def passed_along(value, axis, steps):
    count = lax.axis_size(axis)
    pairs = [(source, (source + steps) % count) for source in range(count)]
    return lax.ppermute(value, axis, pairs)


def chain_part(part, rows, ratings_cols, mask_cols, starts):
    errors = []
    held = []
    for k in range(len(rows)):
        block_rows = rows[k]
        rating_rows = lax.dynamic_slice_in_dim(ratings_cols, starts[k], TILE, 0).astype(jnp.float32)
        observed = lax.dynamic_slice_in_dim(mask_cols, starts[k], TILE, 0).astype(jnp.float32)
        predicted = lax.dot_general(block_rows, part, (((1,), (1,)), ((), ())), precision=HI)
        residual_err = observed * (predicted - rating_rows)
        errors.append(residual_err)
        held.append(part)
        grad_items = lax.dot_general(
            residual_err, block_rows, (((0,), (0,)), ((), ())), precision=HI
        )
        part = part - learning_rate * grad_items
    return part, errors, held


def graph_target(own_block, offsets, count_used, tile_collection):
    user_rows, rank_width = own_block.shape
    sub_count = user_rows // TILE
    half_span = lax.axis_size("users") // 2
    sources = ((-half_span, half_span), (2, -2), (1, -1), (-1, 1))
    total_sum = None
    for steps, offset in sources:
        neighbour = passed_along(own_block, "users", steps).reshape(sub_count, TILE, rank_width)
        picked = (offsets == offset) & (jnp.arange(MAX_LINKS) < count_used)
        mixing = jnp.sum(
            jnp.where(picked[:, None, None, None], tile_collection, 0.0), axis=0
        )
        mixed_rows = jnp.einsum("gcj,gjz->gcz", mixing, neighbour, precision=HI)
        total_sum = mixed_rows if total_sum is None else total_sum + mixed_rows
    return total_sum.reshape(user_rows, rank_width) / count_used.astype(jnp.float32)


def shards(
    user_factors,
    item_factor_blocks,
    ratings,
    rated_mask,
    neighbor_offsets,
    neighbor_counts,
    mix_tiles,
    plan,
):
    own_block = user_factors[0, 0]
    user_rows = own_block.shape[0]
    sub_count = user_rows // TILE
    target = graph_target(own_block, neighbor_offsets[0, 0], neighbor_counts[0, 0], mix_tiles[0, 0])

    item_block = item_factor_blocks[0, 0]
    width = item_block.shape[0] // CHUNKS
    user_now = own_block
    parts = [item_block[c * width:(c + 1) * width] for c in range(CHUNKS)]
    for stop_num in range(STOPS):
        stop_ratings = ratings[0, 0, stop_num]
        halting_mask = rated_mask[0, 0, stop_num]
        starts = [plan[stop_num, k] * TILE for k in range(sub_count)]
        rows = [lax.dynamic_slice_in_dim(user_now, s, TILE, 0) for s in starts]
        last = stop_num == STOPS - 1
        errors = []
        held = []
        for c in range(CHUNKS):
            cols = slice(c * width, (c + 1) * width)
            part, errs, hs = chain_part(
                parts[c], rows, stop_ratings[:, cols], halting_mask[:, cols], starts
            )
            errors.append(errs)
            held.append(hs)
            parts[c] = part if last else passed_along(part, "items", 1)
        for k in range(sub_count):
            block_rows = rows[k]
            grad_users = graph_weight * block_rows
            if stop_num > 0:
                grad_users = grad_users - graph_weight * lax.dynamic_slice_in_dim(
                    target, starts[k], TILE, 0
                )
            for c in range(CHUNKS):
                grad_users = grad_users + jnp.dot(errors[c][k], held[c][k], precision=HI)
            user_now = lax.dynamic_update_slice_in_dim(
                user_now, block_rows - learning_rate * grad_users, starts[k], 0
            )
        if stop_num == 0:
            user_now = user_now + (learning_rate * graph_weight) * target
    item_now = jnp.concatenate(parts, axis=0)
    return (user_now[None, None], item_now[None, None])


def solution(mesh):
    return jax.shard_map(
        shards,
        mesh=mesh,
        in_specs=(
            P("users", "items", None, None),
            P("users", "items", None, None),
            P("users", "items", None, None, None),
            P("users", "items", None, None, None),
            P("users", "items", None),
            P("users", "items"),
            P("users", "items", None, None, None, None),
            P(),
        ),
        out_specs=(P("users", "items", None, None), P("users", "items", None, None)),
        check_vma=False,
    )
```

```python
import jax
import jax.numpy as jnp
from jax import lax
from jax.sharding import PartitionSpec as P

TILE = 128
MAX_LINKS = 4
STOPS = 8
CHUNKS = 1


learning_rate = 0.025
graph_weight = 2.0
HI = lax.Precision.HIGHEST
STEP = lax.Precision.HIGH


def passed_along(value, axis, steps):
    count = lax.axis_size(axis)
    pairs = [(source, (source + steps) % count) for source in range(count)]
    return lax.ppermute(value, axis, pairs)


def chain_part(part, rows, ratings_cols, mask_cols, starts):
    errors = []
    held = []
    for k in range(len(rows)):
        block_rows = rows[k]
        rating_rows = lax.dynamic_slice_in_dim(ratings_cols, starts[k], TILE, 0).astype(jnp.float32)
        observed = lax.dynamic_slice_in_dim(mask_cols, starts[k], TILE, 0).astype(jnp.float32)
        predicted = lax.dot_general(block_rows, part, (((1,), (1,)), ((), ())), precision=STEP)
        residual_err = observed * (predicted - rating_rows)
        errors.append(residual_err)
        held.append(part)
        grad_items = lax.dot_general(
            residual_err, block_rows, (((0,), (0,)), ((), ())), precision=STEP
        )
        part = part - learning_rate * grad_items
    return part, errors, held


def graph_target(own_block, offsets, count_used, tile_collection):
    user_rows, rank_width = own_block.shape
    sub_count = user_rows // TILE
    half_span = lax.axis_size("users") // 2
    sources = ((-half_span, half_span), (2, -2), (1, -1), (-1, 1))
    neighbours = [passed_along(own_block, "users", steps) for steps, _ in sources]
    mixings = []
    for _, offset in sources:
        picked = (offsets == offset) & (jnp.arange(MAX_LINKS) < count_used)
        mixings.append(
            jnp.sum(jnp.where(picked[:, None, None, None], tile_collection, 0.0), axis=0)
        )
    mixings = lax.optimization_barrier(mixings)
    total_sum = None
    for neighbour, mixing in zip(neighbours, mixings):
        neighbour = neighbour.reshape(sub_count, TILE, rank_width)
        mixed_rows = jnp.einsum("gcj,gjz->gcz", mixing, neighbour, precision=HI)
        total_sum = mixed_rows if total_sum is None else total_sum + mixed_rows
    return total_sum.reshape(user_rows, rank_width) / count_used.astype(jnp.float32)


def shards(
    user_factors,
    item_factor_blocks,
    ratings,
    rated_mask,
    neighbor_offsets,
    neighbor_counts,
    mix_tiles,
    plan,
):
    own_block = user_factors[0, 0]
    user_rows = own_block.shape[0]
    sub_count = user_rows // TILE
    target = graph_target(own_block, neighbor_offsets[0, 0], neighbor_counts[0, 0], mix_tiles[0, 0])

    item_block = item_factor_blocks[0, 0]
    width = item_block.shape[0] // CHUNKS
    user_now = own_block
    parts = [item_block[c * width:(c + 1) * width] for c in range(CHUNKS)]
    for stop_num in range(STOPS):
        stop_ratings = ratings[0, 0, stop_num]
        halting_mask = rated_mask[0, 0, stop_num]
        starts = [plan[stop_num, k] * TILE for k in range(sub_count)]
        rows = [lax.dynamic_slice_in_dim(user_now, s, TILE, 0) for s in starts]
        last = stop_num == STOPS - 1
        errors = []
        held = []
        for c in range(CHUNKS):
            cols = slice(c * width, (c + 1) * width)
            part, errs, hs = chain_part(
                parts[c], rows, stop_ratings[:, cols], halting_mask[:, cols], starts
            )
            errors.append(errs)
            held.append(hs)
            parts[c] = part if last else passed_along(part, "items", 1)
        for k in range(sub_count):
            block_rows = rows[k]
            grad_users = graph_weight * block_rows
            if stop_num > 0:
                grad_users = grad_users - graph_weight * lax.dynamic_slice_in_dim(
                    target, starts[k], TILE, 0
                )
            for c in range(CHUNKS):
                grad_users = grad_users + jnp.dot(errors[c][k], held[c][k], precision=STEP)
            user_now = lax.dynamic_update_slice_in_dim(
                user_now, block_rows - learning_rate * grad_users, starts[k], 0
            )
        if stop_num == 0:
            user_now = user_now + (learning_rate * graph_weight) * target
    item_now = jnp.concatenate(parts, axis=0)
    return (user_now[None, None], item_now[None, None])


def solution(mesh):
    return jax.shard_map(
        shards,
        mesh=mesh,
        in_specs=(
            P("users", "items", None, None),
            P("users", "items", None, None),
            P("users", "items", None, None, None),
            P("users", "items", None, None, None),
            P("users", "items", None),
            P("users", "items"),
            P("users", "items", None, None, None, None),
            P(),
        ),
        out_specs=(P("users", "items", None, None), P("users", "items", None, None)),
        check_vma=False,
    )
```

```python
import jax
import jax.numpy as jnp
from jax import lax
from jax.sharding import PartitionSpec as P

TILE = 128
MAX_LINKS = 4
STOPS = 8
CHUNKS = 1


learning_rate = 0.025
graph_weight = 2.0
HI = lax.Precision.HIGHEST
STEP = lax.Precision.HIGH


def passed_along(value, axis, steps):
    count = lax.axis_size(axis)
    pairs = [(source, (source + steps) % count) for source in range(count)]
    return lax.ppermute(value, axis, pairs)


def chain_part(part, rows, ratings_cols, mask_cols, starts):
    errors = []
    held = []
    for k in range(len(rows)):
        block_rows = rows[k]
        rating_rows = lax.dynamic_slice_in_dim(ratings_cols, starts[k], TILE, 0).astype(jnp.float32)
        observed = lax.dynamic_slice_in_dim(mask_cols, starts[k], TILE, 0).astype(jnp.float32)
        predicted = lax.dot_general(block_rows, part, (((1,), (1,)), ((), ())), precision=STEP)
        residual_err = observed * (predicted - rating_rows)
        errors.append(residual_err)
        held.append(part)
        grad_items = lax.dot_general(
            residual_err, block_rows, (((0,), (0,)), ((), ())), precision=STEP
        )
        part = part - learning_rate * grad_items
    return part, errors, held


def graph_target(own_block, offsets, count_used, tile_collection):
    user_rows, rank_width = own_block.shape
    sub_count = user_rows // TILE
    half_span = lax.axis_size("users") // 2
    sources = ((-half_span, half_span), (2, -2), (1, -1), (-1, 1))
    neighbours = [passed_along(own_block, "users", steps) for steps, _ in sources]
    mixings = []
    for _, offset in sources:
        picked = (offsets == offset) & (jnp.arange(MAX_LINKS) < count_used)
        mixings.append(
            jnp.sum(jnp.where(picked[:, None, None, None], tile_collection, 0.0), axis=0)
        )
    stacked = jnp.stack(neighbours).reshape(len(sources), sub_count, TILE, rank_width)
    total_sum = jnp.einsum("bgcj,bgjz->gcz", jnp.stack(mixings), stacked, precision=STEP)
    return total_sum.reshape(user_rows, rank_width) / count_used.astype(jnp.float32)


def shards(
    user_factors,
    item_factor_blocks,
    ratings,
    rated_mask,
    neighbor_offsets,
    neighbor_counts,
    mix_tiles,
    plan,
):
    own_block = user_factors[0, 0]
    user_rows = own_block.shape[0]
    sub_count = user_rows // TILE
    target = graph_target(own_block, neighbor_offsets[0, 0], neighbor_counts[0, 0], mix_tiles[0, 0])

    item_block = item_factor_blocks[0, 0]
    width = item_block.shape[0] // CHUNKS
    user_now = own_block
    parts = [item_block[c * width:(c + 1) * width] for c in range(CHUNKS)]
    for stop_num in range(STOPS):
        stop_ratings = ratings[0, 0, stop_num]
        halting_mask = rated_mask[0, 0, stop_num]
        starts = [plan[stop_num, k] * TILE for k in range(sub_count)]
        rows = [lax.dynamic_slice_in_dim(user_now, s, TILE, 0) for s in starts]
        last = stop_num == STOPS - 1
        errors = []
        held = []
        for c in range(CHUNKS):
            cols = slice(c * width, (c + 1) * width)
            part, errs, hs = chain_part(
                parts[c], rows, stop_ratings[:, cols], halting_mask[:, cols], starts
            )
            errors.append(errs)
            held.append(hs)
            parts[c] = part if last else passed_along(part, "items", 1)
        for k in range(sub_count):
            block_rows = rows[k]
            grad_users = graph_weight * block_rows
            if stop_num > 0:
                grad_users = grad_users - graph_weight * lax.dynamic_slice_in_dim(
                    target, starts[k], TILE, 0
                )
            for c in range(CHUNKS):
                grad_users = grad_users + jnp.dot(errors[c][k], held[c][k], precision=STEP)
            user_now = lax.dynamic_update_slice_in_dim(
                user_now, block_rows - learning_rate * grad_users, starts[k], 0
            )
        if stop_num == 0:
            user_now = user_now + (learning_rate * graph_weight) * target
    item_now = jnp.concatenate(parts, axis=0)
    return (user_now[None, None], item_now[None, None])


def solution(mesh):
    return jax.shard_map(
        shards,
        mesh=mesh,
        in_specs=(
            P("users", "items", None, None),
            P("users", "items", None, None),
            P("users", "items", None, None, None),
            P("users", "items", None, None, None),
            P("users", "items", None),
            P("users", "items"),
            P("users", "items", None, None, None, None),
            P(),
        ),
        out_specs=(P("users", "items", None, None), P("users", "items", None, None)),
        check_vma=False,
    )
```

```python
import jax
import jax.numpy as jnp
from jax import lax
from jax.sharding import PartitionSpec as P

TILE = 128
MAX_LINKS = 4
STOPS = 8
CHUNKS = 1


learning_rate = 0.025
graph_weight = 2.0
HI = lax.Precision.HIGHEST
STEP = lax.Precision.HIGH


def passed_along(value, axis, steps):
    count = lax.axis_size(axis)
    pairs = [(source, (source + steps) % count) for source in range(count)]
    return lax.ppermute(value, axis, pairs)


def chain_part(part, rows, ratings_cols, mask_cols, starts):
    errors = []
    held = []
    for k in range(len(rows)):
        block_rows = rows[k]
        rating_rows = lax.dynamic_slice_in_dim(ratings_cols, starts[k], TILE, 0).astype(jnp.float32)
        observed = lax.dynamic_slice_in_dim(mask_cols, starts[k], TILE, 0).astype(jnp.float32)
        predicted = lax.dot_general(block_rows, part, (((1,), (1,)), ((), ())), precision=STEP)
        residual_err = observed * (predicted - rating_rows)
        errors.append(residual_err)
        held.append(part)
        grad_items = lax.dot_general(
            residual_err, block_rows, (((0,), (0,)), ((), ())), precision=STEP
        )
        part = part - learning_rate * grad_items
    return part, errors, held


def graph_target(own_block, offsets, count_used, tile_collection):
    user_rows, rank_width = own_block.shape
    sub_count = user_rows // TILE
    half_span = lax.axis_size("users") // 2
    sources = ((-half_span, half_span), (2, -2), (1, -1), (-1, 1))
    far_block = passed_along(own_block, "users", -half_span)
    minus_two = passed_along(own_block, "users", 2)
    plus_one = passed_along(own_block, "users", -1)
    count = lax.axis_size("users")
    odd = lax.axis_index("users") % 2 == 1
    relay = jnp.where(odd, minus_two, own_block)
    minus_one = lax.ppermute(relay, "users", [(s, s ^ 1) for s in range(count)])
    neighbours = [far_block, minus_two, minus_one, plus_one]
    mixings = []
    for _, offset in sources:
        picked = (offsets == offset) & (jnp.arange(MAX_LINKS) < count_used)
        mixings.append(
            jnp.sum(jnp.where(picked[:, None, None, None], tile_collection, 0.0), axis=0)
        )
    stacked = jnp.stack(neighbours).reshape(len(sources), sub_count, TILE, rank_width)
    total_sum = jnp.einsum("bgcj,bgjz->gcz", jnp.stack(mixings), stacked, precision=STEP)
    return total_sum.reshape(user_rows, rank_width) / count_used.astype(jnp.float32)


def shards(
    user_factors,
    item_factor_blocks,
    ratings,
    rated_mask,
    neighbor_offsets,
    neighbor_counts,
    mix_tiles,
    plan,
):
    own_block = user_factors[0, 0]
    user_rows = own_block.shape[0]
    sub_count = user_rows // TILE
    target = graph_target(own_block, neighbor_offsets[0, 0], neighbor_counts[0, 0], mix_tiles[0, 0])

    item_block = item_factor_blocks[0, 0]
    width = item_block.shape[0] // CHUNKS
    user_now = own_block
    parts = [item_block[c * width:(c + 1) * width] for c in range(CHUNKS)]
    for stop_num in range(STOPS):
        stop_ratings = ratings[0, 0, stop_num]
        halting_mask = rated_mask[0, 0, stop_num]
        starts = [plan[stop_num, k] * TILE for k in range(sub_count)]
        rows = [lax.dynamic_slice_in_dim(user_now, s, TILE, 0) for s in starts]
        last = stop_num == STOPS - 1
        errors = []
        held = []
        for c in range(CHUNKS):
            cols = slice(c * width, (c + 1) * width)
            part, errs, hs = chain_part(
                parts[c], rows, stop_ratings[:, cols], halting_mask[:, cols], starts
            )
            errors.append(errs)
            held.append(hs)
            parts[c] = part if last else passed_along(part, "items", 1)
        for k in range(sub_count):
            block_rows = rows[k]
            grad_users = graph_weight * block_rows
            if stop_num > 0:
                grad_users = grad_users - graph_weight * lax.dynamic_slice_in_dim(
                    target, starts[k], TILE, 0
                )
            for c in range(CHUNKS):
                grad_users = grad_users + jnp.dot(errors[c][k], held[c][k], precision=STEP)
            user_now = lax.dynamic_update_slice_in_dim(
                user_now, block_rows - learning_rate * grad_users, starts[k], 0
            )
        if stop_num == 0:
            user_now = user_now + (learning_rate * graph_weight) * target
    item_now = jnp.concatenate(parts, axis=0)
    return (user_now[None, None], item_now[None, None])


def solution(mesh):
    return jax.shard_map(
        shards,
        mesh=mesh,
        in_specs=(
            P("users", "items", None, None),
            P("users", "items", None, None),
            P("users", "items", None, None, None),
            P("users", "items", None, None, None),
            P("users", "items", None),
            P("users", "items"),
            P("users", "items", None, None, None, None),
            P(),
        ),
        out_specs=(P("users", "items", None, None), P("users", "items", None, None)),
        check_vma=False,
    )
```

```python
import jax
import jax.numpy as jnp
from jax import lax
from jax.sharding import PartitionSpec as P

TILE = 128
MAX_LINKS = 4
STOPS = 8
CHUNKS = 1


learning_rate = 0.025
graph_weight = 2.0
HI = lax.Precision.HIGHEST
STEP = lax.Precision.HIGH


def passed_along(value, axis, steps):
    count = lax.axis_size(axis)
    pairs = [(source, (source + steps) % count) for source in range(count)]
    return lax.ppermute(value, axis, pairs)


def chain_part(part, rows, ratings_cols, mask_cols, starts):
    errors = []
    held = []
    for k in range(len(rows)):
        block_rows = rows[k]
        rating_rows = lax.dynamic_slice_in_dim(ratings_cols, starts[k], TILE, 0).astype(jnp.float32)
        observed = lax.dynamic_slice_in_dim(mask_cols, starts[k], TILE, 0).astype(jnp.float32)
        predicted = lax.dot_general(block_rows, part, (((1,), (1,)), ((), ())), precision=STEP)
        residual_err = observed * (predicted - rating_rows)
        errors.append(residual_err)
        held.append(part)
        grad_items = lax.dot_general(
            residual_err, block_rows, (((0,), (0,)), ((), ())), precision=STEP
        )
        part = part - learning_rate * grad_items
    return part, errors, held


def graph_target(own_block, offsets, count_used, tile_collection):
    user_rows, rank_width = own_block.shape
    sub_count = user_rows // TILE
    half_span = lax.axis_size("users") // 2
    sources = ((-half_span, half_span), (2, -2), (1, -1), (-1, 1))
    quarter = half_span // 2
    split = (5 * user_rows) // 8
    one_way = passed_along(passed_along(own_block[:split], "users", -quarter), "users", -quarter)
    other_way = passed_along(passed_along(own_block[split:], "users", quarter), "users", quarter)
    far_block = jnp.concatenate([one_way, other_way], axis=0)
    neighbours = [far_block] + [passed_along(own_block, "users", steps) for steps, _ in sources[1:]]
    mixings = []
    for _, offset in sources:
        picked = (offsets == offset) & (jnp.arange(MAX_LINKS) < count_used)
        mixings.append(
            jnp.sum(jnp.where(picked[:, None, None, None], tile_collection, 0.0), axis=0)
        )
    stacked = jnp.stack(neighbours).reshape(len(sources), sub_count, TILE, rank_width)
    total_sum = jnp.einsum("bgcj,bgjz->gcz", jnp.stack(mixings), stacked, precision=STEP)
    return total_sum.reshape(user_rows, rank_width) / count_used.astype(jnp.float32)


def shards(
    user_factors,
    item_factor_blocks,
    ratings,
    rated_mask,
    neighbor_offsets,
    neighbor_counts,
    mix_tiles,
    plan,
):
    own_block = user_factors[0, 0]
    user_rows = own_block.shape[0]
    sub_count = user_rows // TILE
    target = graph_target(own_block, neighbor_offsets[0, 0], neighbor_counts[0, 0], mix_tiles[0, 0])

    item_block = item_factor_blocks[0, 0]
    width = item_block.shape[0] // CHUNKS
    user_now = own_block
    parts = [item_block[c * width:(c + 1) * width] for c in range(CHUNKS)]
    for stop_num in range(STOPS):
        stop_ratings = ratings[0, 0, stop_num]
        halting_mask = rated_mask[0, 0, stop_num]
        starts = [plan[stop_num, k] * TILE for k in range(sub_count)]
        rows = [lax.dynamic_slice_in_dim(user_now, s, TILE, 0) for s in starts]
        last = stop_num == STOPS - 1
        errors = []
        held = []
        for c in range(CHUNKS):
            cols = slice(c * width, (c + 1) * width)
            part, errs, hs = chain_part(
                parts[c], rows, stop_ratings[:, cols], halting_mask[:, cols], starts
            )
            errors.append(errs)
            held.append(hs)
            parts[c] = part if last else passed_along(part, "items", 1)
        for k in range(sub_count):
            block_rows = rows[k]
            grad_users = graph_weight * block_rows
            if stop_num > 0:
                grad_users = grad_users - graph_weight * lax.dynamic_slice_in_dim(
                    target, starts[k], TILE, 0
                )
            for c in range(CHUNKS):
                grad_users = grad_users + jnp.dot(errors[c][k], held[c][k], precision=STEP)
            user_now = lax.dynamic_update_slice_in_dim(
                user_now, block_rows - learning_rate * grad_users, starts[k], 0
            )
        if stop_num == 0:
            user_now = user_now + (learning_rate * graph_weight) * target
    item_now = jnp.concatenate(parts, axis=0)
    return (user_now[None, None], item_now[None, None])


def solution(mesh):
    return jax.shard_map(
        shards,
        mesh=mesh,
        in_specs=(
            P("users", "items", None, None),
            P("users", "items", None, None),
            P("users", "items", None, None, None),
            P("users", "items", None, None, None),
            P("users", "items", None),
            P("users", "items"),
            P("users", "items", None, None, None, None),
            P(),
        ),
        out_specs=(P("users", "items", None, None), P("users", "items", None, None)),
        check_vma=False,
    )
```

```python
import jax
import jax.numpy as jnp
from jax import lax
from jax.sharding import PartitionSpec as P

TILE = 128
MAX_LINKS = 4
STOPS = 8
CHUNKS = 1


learning_rate = 0.025
graph_weight = 2.0
HI = lax.Precision.HIGHEST
STEP = lax.Precision.HIGH


def passed_along(value, axis, steps):
    count = lax.axis_size(axis)
    pairs = [(source, (source + steps) % count) for source in range(count)]
    return lax.ppermute(value, axis, pairs)


def chain_part(part, rows, ratings_cols, mask_cols, starts):
    errors = []
    held = []
    for k in range(len(rows)):
        block_rows = rows[k]
        rating_rows = lax.dynamic_slice_in_dim(ratings_cols, starts[k], TILE, 0).astype(jnp.float32)
        observed = lax.dynamic_slice_in_dim(mask_cols, starts[k], TILE, 0).astype(jnp.float32)
        predicted = lax.dot_general(block_rows, part, (((1,), (1,)), ((), ())), precision=STEP)
        residual_err = observed * (predicted - rating_rows)
        errors.append(residual_err)
        held.append(part)
        grad_items = lax.dot_general(
            residual_err, block_rows, (((0,), (0,)), ((), ())), precision=STEP
        )
        part = part - learning_rate * grad_items
    return part, errors, held


def graph_target(own_block, offsets, count_used, tile_collection):
    user_rows, rank_width = own_block.shape
    sub_count = user_rows // TILE
    half_span = lax.axis_size("users") // 2
    sources = ((-half_span, half_span), (2, -2), (1, -1), (-1, 1))
    neighbours = [passed_along(own_block, "users", steps) for steps, _ in sources]
    mixings = []
    for _, offset in sources:
        picked = (offsets == offset) & (jnp.arange(MAX_LINKS) < count_used)
        mixings.append(
            jnp.sum(jnp.where(picked[:, None, None, None], tile_collection, 0.0), axis=0)
        )
    stacked = jnp.concatenate(
        [n.reshape(sub_count, TILE, rank_width) for n in neighbours], axis=1
    )
    mixing = jnp.concatenate(mixings, axis=2)
    total_sum = jnp.einsum("gck,gkz->gcz", mixing, stacked, precision=STEP)
    return total_sum.reshape(user_rows, rank_width) / count_used.astype(jnp.float32)


def shards(
    user_factors,
    item_factor_blocks,
    ratings,
    rated_mask,
    neighbor_offsets,
    neighbor_counts,
    mix_tiles,
    plan,
):
    own_block = user_factors[0, 0]
    user_rows = own_block.shape[0]
    sub_count = user_rows // TILE
    target = graph_target(own_block, neighbor_offsets[0, 0], neighbor_counts[0, 0], mix_tiles[0, 0])

    item_block = item_factor_blocks[0, 0]
    width = item_block.shape[0] // CHUNKS
    user_now = own_block
    parts = [item_block[c * width:(c + 1) * width] for c in range(CHUNKS)]
    for stop_num in range(STOPS):
        stop_ratings = ratings[0, 0, stop_num]
        halting_mask = rated_mask[0, 0, stop_num]
        starts = [plan[stop_num, k] * TILE for k in range(sub_count)]
        rows = [lax.dynamic_slice_in_dim(user_now, s, TILE, 0) for s in starts]
        last = stop_num == STOPS - 1
        errors = []
        held = []
        for c in range(CHUNKS):
            cols = slice(c * width, (c + 1) * width)
            part, errs, hs = chain_part(
                parts[c], rows, stop_ratings[:, cols], halting_mask[:, cols], starts
            )
            errors.append(errs)
            held.append(hs)
            parts[c] = part if last else passed_along(part, "items", 1)
        for k in range(sub_count):
            block_rows = rows[k]
            grad_users = graph_weight * block_rows
            if stop_num > 0:
                grad_users = grad_users - graph_weight * lax.dynamic_slice_in_dim(
                    target, starts[k], TILE, 0
                )
            for c in range(CHUNKS):
                grad_users = grad_users + jnp.dot(errors[c][k], held[c][k], precision=STEP)
            user_now = lax.dynamic_update_slice_in_dim(
                user_now, block_rows - learning_rate * grad_users, starts[k], 0
            )
        if stop_num == 0:
            user_now = user_now + (learning_rate * graph_weight) * target
    item_now = jnp.concatenate(parts, axis=0)
    return (user_now[None, None], item_now[None, None])


def solution(mesh):
    return jax.shard_map(
        shards,
        mesh=mesh,
        in_specs=(
            P("users", "items", None, None),
            P("users", "items", None, None),
            P("users", "items", None, None, None),
            P("users", "items", None, None, None),
            P("users", "items", None),
            P("users", "items"),
            P("users", "items", None, None, None, None),
            P(),
        ),
        out_specs=(P("users", "items", None, None), P("users", "items", None, None)),
        check_vma=False,
    )
```

```python
import jax
import jax.numpy as jnp
from jax import lax
from jax.sharding import PartitionSpec as P

TILE = 128
MAX_LINKS = 4
STOPS = 8
CHUNKS = 1


learning_rate = 0.025
graph_weight = 2.0
HI = lax.Precision.HIGHEST
STEP = lax.Precision.HIGH


def passed_along(value, axis, steps):
    count = lax.axis_size(axis)
    pairs = [(source, (source + steps) % count) for source in range(count)]
    return lax.ppermute(value, axis, pairs)


def chain_part(part, rows, ratings_cols, mask_cols, starts):
    errors = []
    held = []
    for k in range(len(rows)):
        block_rows = rows[k]
        rating_rows = lax.dynamic_slice_in_dim(ratings_cols, starts[k], TILE, 0).astype(jnp.float32)
        observed = lax.dynamic_slice_in_dim(mask_cols, starts[k], TILE, 0).astype(jnp.float32)
        predicted = lax.dot_general(block_rows, part, (((1,), (1,)), ((), ())), precision=STEP)
        residual_err = observed * (predicted - rating_rows)
        errors.append(residual_err)
        held.append(part)
        grad_items = lax.dot_general(
            residual_err, block_rows, (((0,), (0,)), ((), ())), precision=STEP
        )
        part = part - learning_rate * grad_items
    return part, errors, held


def graph_target(own_block, offsets, count_used, tile_collection):
    user_rows, rank_width = own_block.shape
    sub_count = user_rows // TILE
    half_span = lax.axis_size("users") // 2
    sources = ((-half_span, half_span), (2, -2), (1, -1), (-1, 1))
    neighbours = [passed_along(own_block, "users", steps) for steps, _ in sources]
    mixings = []
    for _, offset in sources:
        picked = (offsets == offset) & (jnp.arange(MAX_LINKS) < count_used)
        mixings.append(
            jnp.sum(jnp.where(picked[:, None, None, None], tile_collection, 0.0), axis=0)
        )
    stacked = jnp.stack(neighbours).reshape(len(sources), sub_count, TILE, rank_width)
    total_sum = jnp.einsum("bgcj,bgjz->gcz", jnp.stack(mixings), stacked, precision=STEP)
    return total_sum.reshape(user_rows, rank_width) / count_used.astype(jnp.float32)


def shards(
    user_factors,
    item_factor_blocks,
    ratings,
    rated_mask,
    neighbor_offsets,
    neighbor_counts,
    mix_tiles,
    plan,
):
    own_block = user_factors[0, 0]
    user_rows = own_block.shape[0]
    sub_count = user_rows // TILE
    target = graph_target(own_block, neighbor_offsets[0, 0], neighbor_counts[0, 0], mix_tiles[0, 0])

    item_block = item_factor_blocks[0, 0]
    width = item_block.shape[0] // CHUNKS
    user_now = own_block
    parts = [item_block[c * width:(c + 1) * width] for c in range(CHUNKS)]
    for stop_num in range(STOPS):
        stop_ratings = ratings[0, 0, stop_num]
        halting_mask = rated_mask[0, 0, stop_num]
        starts = [plan[stop_num, k] * TILE for k in range(sub_count)]
        if stop_num == 1:
            rows = [
                lax.dynamic_slice_in_dim(goal_free, s, TILE, 0)
                + (learning_rate * graph_weight) * lax.dynamic_slice_in_dim(target, s, TILE, 0)
                for s in starts
            ]
        else:
            rows = [lax.dynamic_slice_in_dim(user_now, s, TILE, 0) for s in starts]
        last = stop_num == STOPS - 1
        errors = []
        held = []
        for c in range(CHUNKS):
            cols = slice(c * width, (c + 1) * width)
            part, errs, hs = chain_part(
                parts[c], rows, stop_ratings[:, cols], halting_mask[:, cols], starts
            )
            errors.append(errs)
            held.append(hs)
            parts[c] = part if last else passed_along(part, "items", 1)
        for k in range(sub_count):
            block_rows = rows[k]
            grad_users = graph_weight * block_rows
            if stop_num > 0:
                grad_users = grad_users - graph_weight * lax.dynamic_slice_in_dim(
                    target, starts[k], TILE, 0
                )
            for c in range(CHUNKS):
                grad_users = grad_users + jnp.dot(errors[c][k], held[c][k], precision=STEP)
            user_now = lax.dynamic_update_slice_in_dim(
                user_now, block_rows - learning_rate * grad_users, starts[k], 0
            )
        if stop_num == 0:
            goal_free = user_now
            user_now = user_now + (learning_rate * graph_weight) * target
    item_now = jnp.concatenate(parts, axis=0)
    return (user_now[None, None], item_now[None, None])


def solution(mesh):
    return jax.shard_map(
        shards,
        mesh=mesh,
        in_specs=(
            P("users", "items", None, None),
            P("users", "items", None, None),
            P("users", "items", None, None, None),
            P("users", "items", None, None, None),
            P("users", "items", None),
            P("users", "items"),
            P("users", "items", None, None, None, None),
            P(),
        ),
        out_specs=(P("users", "items", None, None), P("users", "items", None, None)),
        check_vma=False,
    )
```
